512 devices in a mesh: req: 128 (over y, z, core), tp: 4 (over x).
Axes of the slice: x: 4, y: 4, z: 16, core: 2. Of those that a mesh axis runs over, the one named last changes fastest.
Arguments:
- tokens: bfloat16 [131072, 3584], P('req', 'tp'), may hold values from -6 to 6
- key_value_weight: bfloat16 [3584, 1024], P('tp'), may hold values from -0.09375 to 0.09375
- adapter_down_maps: bfloat16 [128, 16, 3584], P('req', None, 'tp'), may hold values from -0.09375 to 0.09375
- adapter_up_maps: bfloat16 [128, 16, 1024], P('req', None, 'tp'), may hold values from -1.5 to 1.5
- block_adapter_ids: int32 [1024], P('req'), may hold values from 0 to 127, never falling along the last dimension, each value on 1 to 32 neighbouring positions
- block_live_rows: int32 [1024], P('req'), may hold values from 32 to 128
- adapter_storage_slot: int32 [128], replicated, may hold values from 0 to 127, each once
Outputs:
- keys_values: bfloat16 [131072, 1024], P('req', 'tp')
The draws below stay inside these ranges and needn't reach their ends.
Inputs may be any that keep to these rules, and one draw needn't show every extreme that they name: `block_adapter_ids`: block ids never fall from one block to the next, every adapter id names at least one block, and one adapter names 32 blocks. `adapter_storage_slot`: each storage slot belongs to exactly one adapter.
All inputs are finite; a program needn't handle non-finite values.
Results may differ from the reference program's by a relative error of at most 0.003.
Values may be sent and summed in bfloat16 or wider, within the bound.
No kernel may reach another device: no remote copies, remote signals or barrier semaphores. Data moves between devices by JAX's collectives and lax.ppermute only.
A program may use at most 64 MiB of HBM per device.

```python
import math
import jax
import jax.numpy as jnp
import numpy as np
from jax import lax

MODEL_WIDTH = 3584
ADAPTER_RANK = 16
BLK = 128
KEY_VALUE_COLS = 1024
ADAPTER_TOTAL = 128
BLK_DEV = 8
BLOCKS = 1024
TOKENS = 131072
N_REQ = 128


def place_ends(drawn, own_key, smallest, largest):
    index_at = [jax.random.randint(jax.random.fold_in(own_key, axis), (), 0, length) for axis, length in enumerate(drawn.shape)]
    widest = drawn.shape.index(max(drawn.shape))
    next_to = index_at[:widest] + [(index_at[widest] + 1) % drawn.shape[widest]] + index_at[widest + 1:]
    return drawn.at[tuple(index_at)].set(smallest).at[tuple(next_to)].set(largest)


def block_scale(key, extent, split, least, high):
    factor_of, own = 1.0, jax.random.fold_in(key, 6)
    for axis_at, blocks in split:
        heights = jnp.exp(jax.random.uniform(jax.random.fold_in(own, axis_at), (blocks,), jnp.float32, least / len(split), high / len(split)))
        factor_of = factor_of * jnp.repeat(heights, extent[axis_at] // blocks).reshape([-1 if axis == axis_at else 1 for axis in range(len(extent))])
    return factor_of


def length_profile(count, total, reach, lean):
    weights = [(1 << 20) // math.isqrt(rank ** lean) + 1 for rank in range(2, count + 1)]
    surplus, given = total - reach - (count - 1), [1] * (count - 1)
    while surplus > 0:
        candidates = [i for i in range(count - 1) if given[i] < reach]
        whole, remaining = sum([weights[i] for i in candidates]), surplus
        for i in candidates:
            more = min(reach - given[i], max(1, remaining * weights[i] // whole), surplus)
            given[i] = given[i] + more
            surplus = surplus - more
    return np.array([reach] + given)


def uneven_parts(stream_key, number_of, total, reach, slope):
    if number_of == 2:
        one = jax.random.randint(stream_key, (), max(1, total - reach), min(reach, total - 1) + 1)
        return jnp.stack([one, total - one])
    tallies = jnp.asarray(length_profile(number_of, total, reach, slope), jnp.int32)
    couples = (number_of - 1) // 2
    source_of, sink = tallies[1:1 + 2 * couples:2], tallies[2:2 + 2 * couples:2]
    room = jnp.minimum(source_of - 1, reach - sink)
    passed = jax.random.randint(jax.random.fold_in(stream_key, 1), (couples,), 0, 1 << 20) % (room + 1)
    tallies = tallies.at[1:1 + 2 * couples:2].set(source_of - passed).at[2:2 + 2 * couples:2].set(sink + passed)
    return tallies[jax.random.permutation(jax.random.fold_in(stream_key, 2), number_of)]


def noise(key, extent, width, reach, pieces=(), held_as=jnp.bfloat16):
    loudness = block_scale(key, extent, pieces, -0.22, 0.18) if pieces else 1.0
    values = jax.random.normal(key, extent, jnp.float32) * width * loudness
    return jnp.minimum(jnp.maximum(values, -reach), reach).astype(held_as)


def setup_inputs(seed: int = 0) -> dict:
    splits = jax.random.split(jax.random.key(seed), 8)
    tokens = noise(splits[0], (TOKENS, MODEL_WIDTH), 1.0, 6.0, ((0, 128), (1, 4)))
    key_value_weight = noise(splits[1], (MODEL_WIDTH, KEY_VALUE_COLS), MODEL_WIDTH ** -0.5, 0.09375, ((0, 4),))
    adapter_down_maps = noise(splits[2], (ADAPTER_TOTAL, ADAPTER_RANK, MODEL_WIDTH), MODEL_WIDTH ** -0.5, 0.09375, ((0, 128), (2, 4)))
    adapter_up_maps = noise(splits[3], (ADAPTER_TOTAL, ADAPTER_RANK, KEY_VALUE_COLS), ADAPTER_RANK ** -0.5, 1.5, ((0, 128), (2, 4)))
    block_adapter_ids = jnp.searchsorted(jnp.cumsum(uneven_parts(splits[4], ADAPTER_TOTAL, BLOCKS, 32, 2)), jnp.arange(BLOCKS), side="right").astype(jnp.int32)
    block_live_rows = place_ends(jax.random.randint(splits[5], (BLOCKS,), BLK // 4, BLK + 1), jax.random.fold_in(splits[5], 1), BLK // 4, BLK).astype(jnp.int32)
    adapter_storage_slot = jax.random.permutation(splits[6], ADAPTER_TOTAL).astype(jnp.int32)
    return dict(tokens=tokens, key_value_weight=key_value_weight, adapter_down_maps=adapter_down_maps, adapter_up_maps=adapter_up_maps, block_adapter_ids=block_adapter_ids, block_live_rows=block_live_rows, adapter_storage_slot=adapter_storage_slot)


adapter_scale = 0.5


def reference(tokens, key_value_weight, adapter_down_maps, adapter_up_maps, block_adapter_ids, block_live_rows, adapter_storage_slot):
    slot_ids = adapter_storage_slot[block_adapter_ids].astype(jnp.int32)

    def one_shard(shard_args):
        rows, local_slot_ids, fill_rows = shard_args
        base_result = jnp.dot(rows, key_value_weight, preferred_element_type=jnp.float32)
        blocked_input = rows.reshape(BLK_DEV, BLK, MODEL_WIDTH).astype(jnp.float32)
        chosen_down_maps = adapter_down_maps[local_slot_ids].astype(jnp.float32)
        chosen_up_maps = adapter_up_maps[local_slot_ids].astype(jnp.float32)
        rank_reduced = jnp.einsum('qzo,qjo->qzj', blocked_input, chosen_down_maps)
        rank_reduced = lax.optimization_barrier(rank_reduced.astype(jnp.bfloat16)).astype(jnp.float32)
        adapter_result = jnp.einsum('bkr,brc->bkc', rank_reduced, chosen_up_maps).reshape(BLK_DEV * BLK, KEY_VALUE_COLS)
        live_rows = (jnp.arange(BLK, dtype=jnp.int32)[None, :] < fill_rows[:, None]).reshape(BLK_DEV * BLK, 1)
        adapted_output = base_result + adapter_scale * adapter_result
        return jnp.where(live_rows, adapted_output, jnp.zeros_like(adapted_output)).astype(jnp.bfloat16)

    result = lax.map(one_shard, (tokens.reshape(N_REQ, BLK_DEV * BLK, MODEL_WIDTH),
                                 slot_ids.reshape(N_REQ, BLK_DEV),
                                 block_live_rows.reshape(N_REQ, BLK_DEV)))
    return result.reshape(TOKENS, KEY_VALUE_COLS)
```

```python
import jax
import jax.numpy as jnp
from jax import lax
from jax.sharding import PartitionSpec as P

adapter_scale = 0.5


def shards(
    tokens,
    key_value_weight,
    adapter_down_maps,
    adapter_up_maps,
    block_adapter_ids,
    block_live_rows,
    adapter_storage_slot,
):
    rows_dev, width_dev = tokens.shape
    blocks_dev = block_adapter_ids.shape[0]
    block_rows = rows_dev // blocks_dev
    rank = adapter_down_maps.shape[1]
    local_columns = adapter_up_maps.shape[2]
    tp_size = key_value_weight.shape[1] // local_columns

    slot_ids = adapter_storage_slot[block_adapter_ids]

    both_maps = jnp.concatenate([adapter_down_maps, adapter_up_maps], axis=2)
    all_maps = lax.all_gather(both_maps, "req", axis=0, tiled=True)
    chosen_maps = all_maps[slot_ids]
    chosen_down_maps = chosen_maps[:, :, :width_dev]
    chosen_up_maps = chosen_maps[:, :, width_dev:]

    base_partial = jnp.dot(tokens, key_value_weight, preferred_element_type=jnp.float32)
    blocked_input = tokens.reshape(blocks_dev, block_rows, width_dev)
    shrunk_partial = jnp.einsum(
        "qzo,qjo->qzj", blocked_input, chosen_down_maps, preferred_element_type=jnp.float32
    ).reshape(rows_dev, rank)
    payload = jnp.concatenate(
        [
            base_partial.reshape(rows_dev, tp_size, local_columns).transpose(1, 0, 2),
            jnp.broadcast_to(shrunk_partial[None], (tp_size, rows_dev, rank)),
        ],
        axis=2,
    )
    summed = lax.psum_scatter(payload, "tp", scatter_dimension=0, tiled=False)
    base_result = summed[:, :local_columns]
    low_values = summed[:, local_columns:].astype(jnp.bfloat16)

    adapter_result = jnp.einsum(
        "bkr,brc->bkc",
        low_values.reshape(blocks_dev, block_rows, rank),
        chosen_up_maps,
        preferred_element_type=jnp.float32,
    ).reshape(rows_dev, local_columns)
    live_rows = (
        jnp.arange(block_rows, dtype=jnp.int32)[None, :] < block_live_rows[:, None]
    ).reshape(rows_dev, 1)
    adapted_output = base_result + adapter_scale * adapter_result
    return jnp.where(live_rows, adapted_output, jnp.zeros_like(adapted_output)).astype(jnp.bfloat16)


def solution(mesh):
    in_specs = (
        P("req", "tp"),
        P("tp", None),
        P("req", None, "tp"),
        P("req", None, "tp"),
        P("req"),
        P("req"),
        P(),
    )
    out_specs = P("req", "tp")
    return jax.shard_map(shards, mesh=mesh, in_specs=in_specs, out_specs=out_specs, check_vma=False)
```

```python
import numpy as np

import jax
import jax.numpy as jnp
from jax import lax
from jax.sharding import Mesh
from jax.sharding import PartitionSpec as P

adapter_scale = 0.5
ROWS = ("y", "z", "c")


def pick_entries(table, wanted, own_row, per_row, per_column):
    row_of = wanted // per_row
    inside = wanted % per_row
    entries = table[inside % per_column, inside // per_column]
    keep = (row_of == own_row)[:, None, None]
    return jnp.where(keep, entries, jnp.zeros_like(entries))


def shards(
    tokens,
    key_value_weight,
    adapter_down_maps,
    adapter_up_maps,
    block_adapter_ids,
    block_live_rows,
    adapter_storage_slot,
):
    rows_dev, width_dev = tokens.shape
    blocks_dev = block_adapter_ids.shape[0]
    block_rows = rows_dev // blocks_dev
    rank = adapter_down_maps.shape[1]
    local_columns = adapter_up_maps.shape[2]
    tp_size = key_value_weight.shape[1] // local_columns
    y_size = lax.axis_size("y")
    per_column = lax.axis_size("c")
    per_row = lax.axis_size("z") * per_column

    slot_ids = adapter_storage_slot[block_adapter_ids]
    my_row = lax.axis_index("y")

    base_partial = jnp.dot(tokens, key_value_weight, preferred_element_type=jnp.float32)
    outgoing = base_partial.reshape(rows_dev, tp_size, local_columns).transpose(1, 0, 2)
    incoming = lax.all_to_all(outgoing, "tp", 0, 0, tiled=False)
    base_result = jnp.sum(incoming, axis=0)

    both_maps = jnp.concatenate([adapter_down_maps, adapter_up_maps], axis=2)
    column = lax.all_gather(both_maps, "z", axis=0, tiled=True)
    row_table = lax.all_gather(column, "c", axis=0, tiled=False)
    chosen_maps = pick_entries(row_table, slot_ids, my_row, per_row, per_column)
    for shift in range(1, y_size):
        their_ids = lax.ppermute(
            slot_ids, "y", [(i, (i - shift) % y_size) for i in range(y_size)]
        )
        sent = pick_entries(row_table, their_ids, my_row, per_row, per_column)
        chosen_maps = chosen_maps + lax.ppermute(
            sent, "y", [(i, (i + shift) % y_size) for i in range(y_size)]
        )
    chosen_down_maps = chosen_maps[:, :, :width_dev]
    chosen_up_maps = chosen_maps[:, :, width_dev:]

    blocked_input = tokens.reshape(blocks_dev, block_rows, width_dev)
    shrunk_partial = jnp.einsum(
        "qzo,qjo->qzj", blocked_input, chosen_down_maps, preferred_element_type=jnp.float32
    ).reshape(rows_dev, rank)
    shrunk = jnp.sum(lax.all_gather(shrunk_partial, "tp", axis=0, tiled=False), axis=0)
    low_values = shrunk.astype(jnp.bfloat16)

    adapter_result = jnp.einsum(
        "bkr,brc->bkc",
        low_values.reshape(blocks_dev, block_rows, rank),
        chosen_up_maps,
        preferred_element_type=jnp.float32,
    ).reshape(rows_dev, local_columns)
    live_rows = (
        jnp.arange(block_rows, dtype=jnp.int32)[None, :] < block_live_rows[:, None]
    ).reshape(rows_dev, 1)
    adapted_output = base_result + adapter_scale * adapter_result
    return jnp.where(live_rows, adapted_output, jnp.zeros_like(adapted_output)).astype(jnp.bfloat16)


def split_mesh(mesh):
    devices = np.asarray(mesh.devices)
    first = devices[:, 0]
    y_size = len({d.coords[1] for d in first})
    z_size = len({d.coords[2] for d in first})
    c_size = len({d.core_on_chip for d in first})
    split = devices.reshape(y_size, z_size, c_size, devices.shape[1])
    for (yi, zi, ci), d in np.ndenumerate(split[:, :, :, 0]):
        assert (d.coords[1], d.coords[2], d.core_on_chip) == (
            sorted({e.coords[1] for e in first})[yi],
            sorted({e.coords[2] for e in first})[zi],
            sorted({e.core_on_chip for e in first})[ci],
        )
    return Mesh(split, ROWS + ("tp",))


def solution(mesh):
    in_specs = (
        P(ROWS, "tp"),
        P("tp", None),
        P(ROWS, None, "tp"),
        P(ROWS, None, "tp"),
        P(ROWS),
        P(ROWS),
        P(),
    )
    out_specs = P(ROWS, "tp")
    return jax.shard_map(
        shards, mesh=split_mesh(mesh), in_specs=in_specs, out_specs=out_specs, check_vma=False
    )
```

```python
import numpy as np

import jax
import jax.numpy as jnp
from jax import lax
from jax.sharding import Mesh
from jax.sharding import PartitionSpec as P

adapter_scale = 0.5
ROWS = ("y", "z", "c")


def pick_entries(table, wanted, own_row, per_row, per_column):
    row_of = wanted // per_row
    inside = wanted % per_row
    entries = table[inside % per_column, inside // per_column]
    keep = (row_of == own_row)[:, None, None]
    return jnp.where(keep, entries, jnp.zeros_like(entries))


def shards(
    tokens,
    key_value_weight,
    adapter_down_maps,
    adapter_up_maps,
    block_adapter_ids,
    block_live_rows,
    adapter_storage_slot,
):
    rows_dev, width_dev = tokens.shape
    blocks_dev = block_adapter_ids.shape[0]
    block_rows = rows_dev // blocks_dev
    rank = adapter_down_maps.shape[1]
    local_columns = adapter_up_maps.shape[2]
    tp_size = key_value_weight.shape[1] // local_columns
    y_size = lax.axis_size("y")
    per_column = lax.axis_size("c")
    per_row = lax.axis_size("z") * per_column

    slot_ids = adapter_storage_slot[block_adapter_ids]
    my_row = lax.axis_index("y")

    both_maps = jnp.concatenate([adapter_down_maps, adapter_up_maps], axis=2)
    column = lax.all_gather(both_maps, "z", axis=0, tiled=True)
    tokens, key_value_weight, slot_ids, column = lax.optimization_barrier(
        (tokens, key_value_weight, slot_ids, column)
    )
    row_table = lax.all_gather(column, "c", axis=0, tiled=False)
    row_ids = lax.all_to_all(
        jnp.broadcast_to(slot_ids[None], (y_size, blocks_dev)), "y", 0, 0, tiled=False
    )

    base_partial = jnp.dot(tokens, key_value_weight, preferred_element_type=jnp.float32)
    outgoing = base_partial.reshape(rows_dev, tp_size, local_columns).transpose(1, 0, 2)
    incoming = lax.all_to_all(outgoing, "tp", 0, 0, tiled=False)
    base_result = jnp.sum(incoming, axis=0)

    sent = pick_entries(row_table, row_ids.reshape(-1), my_row, per_row, per_column)
    received = lax.all_to_all(
        sent.reshape((y_size, blocks_dev) + sent.shape[1:]), "y", 0, 0, tiled=False
    )
    chosen_maps = jnp.sum(received, axis=0, dtype=received.dtype)
    chosen_down_maps = chosen_maps[:, :, :width_dev]
    chosen_up_maps = chosen_maps[:, :, width_dev:]

    blocked_input = tokens.reshape(blocks_dev, block_rows, width_dev)
    shrunk_partial = jnp.einsum(
        "qzo,qjo->qzj", blocked_input, chosen_down_maps, preferred_element_type=jnp.float32
    ).reshape(rows_dev, rank)
    shrunk = jnp.sum(lax.all_gather(shrunk_partial, "tp", axis=0, tiled=False), axis=0)
    low_values = shrunk.astype(jnp.bfloat16)

    adapter_result = jnp.einsum(
        "bkr,brc->bkc",
        low_values.reshape(blocks_dev, block_rows, rank),
        chosen_up_maps,
        preferred_element_type=jnp.float32,
    ).reshape(rows_dev, local_columns)
    live_rows = (
        jnp.arange(block_rows, dtype=jnp.int32)[None, :] < block_live_rows[:, None]
    ).reshape(rows_dev, 1)
    adapted_output = base_result + adapter_scale * adapter_result
    return jnp.where(live_rows, adapted_output, jnp.zeros_like(adapted_output)).astype(jnp.bfloat16)


def split_mesh(mesh):
    devices = np.asarray(mesh.devices)
    first = devices[:, 0]
    y_size = len({d.coords[1] for d in first})
    z_size = len({d.coords[2] for d in first})
    c_size = len({d.core_on_chip for d in first})
    split = devices.reshape(y_size, z_size, c_size, devices.shape[1])
    for (yi, zi, ci), d in np.ndenumerate(split[:, :, :, 0]):
        assert (d.coords[1], d.coords[2], d.core_on_chip) == (
            sorted({e.coords[1] for e in first})[yi],
            sorted({e.coords[2] for e in first})[zi],
            sorted({e.core_on_chip for e in first})[ci],
        )
    return Mesh(split, ROWS + ("tp",))


def solution(mesh):
    in_specs = (
        P(ROWS, "tp"),
        P("tp", None),
        P(ROWS, None, "tp"),
        P(ROWS, None, "tp"),
        P(ROWS),
        P(ROWS),
        P(),
    )
    out_specs = P(ROWS, "tp")
    return jax.shard_map(
        shards, mesh=split_mesh(mesh), in_specs=in_specs, out_specs=out_specs, check_vma=False
    )
```

```python
import numpy as np

import jax
import jax.numpy as jnp
from jax import lax
from jax.sharding import Mesh
from jax.sharding import PartitionSpec as P

adapter_scale = 0.5
ROWS = ("y", "z", "c")


def pick_entries(table, wanted, own_row, per_row, per_column):
    row_of = wanted // per_row
    inside = wanted % per_row
    entries = table[inside % per_column, inside // per_column]
    keep = (row_of == own_row)[:, None, None]
    return jnp.where(keep, entries, jnp.zeros_like(entries))


def shards(
    tokens,
    key_value_weight,
    adapter_down_maps,
    adapter_up_maps,
    block_adapter_ids,
    block_live_rows,
    adapter_storage_slot,
):
    rows_dev, width_dev = tokens.shape
    blocks_dev = block_adapter_ids.shape[0]
    block_rows = rows_dev // blocks_dev
    rank = adapter_down_maps.shape[1]
    local_columns = adapter_up_maps.shape[2]
    tp_size = key_value_weight.shape[1] // local_columns
    y_size = lax.axis_size("y")
    per_column = lax.axis_size("c")
    per_row = lax.axis_size("z") * per_column

    slot_ids = adapter_storage_slot[block_adapter_ids]
    my_row = lax.axis_index("y")

    base_partial = jnp.dot(tokens, key_value_weight, preferred_element_type=jnp.float32)
    outgoing = base_partial.reshape(rows_dev, tp_size, local_columns).transpose(1, 0, 2)
    incoming = lax.all_to_all(outgoing, "tp", 0, 0, tiled=False)
    base_result = jnp.sum(incoming, axis=0)

    both_maps = jnp.concatenate([adapter_down_maps, adapter_up_maps], axis=2)
    both_maps, outgoing = lax.optimization_barrier((both_maps, outgoing))
    column = lax.all_gather(both_maps, "z", axis=0, tiled=True)
    row_table = lax.all_gather(column, "c", axis=0, tiled=False)
    row_ids = jnp.stack(
        [slot_ids]
        + [
            lax.ppermute(slot_ids, "y", [(i, (i - shift) % y_size) for i in range(y_size)])
            for shift in range(1, y_size)
        ]
    )
    row_ids = jnp.roll(row_ids, my_row, axis=0)
    row_table, base_result = lax.optimization_barrier((row_table, base_result))

    sent = pick_entries(row_table, row_ids.reshape(-1), my_row, per_row, per_column)
    received = lax.all_to_all(
        sent.reshape((y_size, blocks_dev) + sent.shape[1:]), "y", 0, 0, tiled=False
    )
    chosen_maps = jnp.sum(received, axis=0, dtype=received.dtype)
    chosen_down_maps = chosen_maps[:, :, :width_dev]
    chosen_up_maps = chosen_maps[:, :, width_dev:]

    blocked_input = tokens.reshape(blocks_dev, block_rows, width_dev)
    shrunk_partial = jnp.einsum(
        "qzo,qjo->qzj", blocked_input, chosen_down_maps, preferred_element_type=jnp.float32
    ).reshape(rows_dev, rank)
    shrunk = jnp.sum(lax.all_gather(shrunk_partial, "tp", axis=0, tiled=False), axis=0)
    low_values = shrunk.astype(jnp.bfloat16)

    adapter_result = jnp.einsum(
        "bkr,brc->bkc",
        low_values.reshape(blocks_dev, block_rows, rank),
        chosen_up_maps,
        preferred_element_type=jnp.float32,
    ).reshape(rows_dev, local_columns)
    live_rows = (
        jnp.arange(block_rows, dtype=jnp.int32)[None, :] < block_live_rows[:, None]
    ).reshape(rows_dev, 1)
    adapted_output = base_result + adapter_scale * adapter_result
    return jnp.where(live_rows, adapted_output, jnp.zeros_like(adapted_output)).astype(jnp.bfloat16)


def split_mesh(mesh):
    devices = np.asarray(mesh.devices)
    first = devices[:, 0]
    y_size = len({d.coords[1] for d in first})
    z_size = len({d.coords[2] for d in first})
    c_size = len({d.core_on_chip for d in first})
    split = devices.reshape(y_size, z_size, c_size, devices.shape[1])
    for (yi, zi, ci), d in np.ndenumerate(split[:, :, :, 0]):
        assert (d.coords[1], d.coords[2], d.core_on_chip) == (
            sorted({e.coords[1] for e in first})[yi],
            sorted({e.coords[2] for e in first})[zi],
            sorted({e.core_on_chip for e in first})[ci],
        )
    return Mesh(split, ROWS + ("tp",))


def solution(mesh):
    in_specs = (
        P(ROWS, "tp"),
        P("tp", None),
        P(ROWS, None, "tp"),
        P(ROWS, None, "tp"),
        P(ROWS),
        P(ROWS),
        P(),
    )
    out_specs = P(ROWS, "tp")
    return jax.shard_map(
        shards, mesh=split_mesh(mesh), in_specs=in_specs, out_specs=out_specs, check_vma=False
    )
```

```python
import numpy as np

import jax
import jax.numpy as jnp
from jax import lax
from jax.sharding import Mesh
from jax.sharding import PartitionSpec as P

adapter_scale = 0.5
ROWS = ("y", "z", "c")


def pick_entries(table, wanted, own_row, per_row, per_column):
    row_of = wanted // per_row
    inside = wanted % per_row
    entries = table[inside % per_column, inside // per_column]
    keep = (row_of == own_row)[:, None, None]
    return jnp.where(keep, entries, jnp.zeros_like(entries))


def shards(
    tokens,
    key_value_weight,
    adapter_down_maps,
    adapter_up_maps,
    block_adapter_ids,
    block_live_rows,
    adapter_storage_slot,
):
    rows_dev, width_dev = tokens.shape
    blocks_dev = block_adapter_ids.shape[0]
    block_rows = rows_dev // blocks_dev
    rank = adapter_down_maps.shape[1]
    local_columns = adapter_up_maps.shape[2]
    tp_size = key_value_weight.shape[1] // local_columns
    y_size = lax.axis_size("y")
    per_column = lax.axis_size("c")
    per_row = lax.axis_size("z") * per_column

    slot_ids = adapter_storage_slot[block_adapter_ids]
    my_row = lax.axis_index("y")

    base_partial = jnp.dot(tokens, key_value_weight, preferred_element_type=jnp.float32)
    outgoing = base_partial.reshape(rows_dev, tp_size, local_columns).transpose(1, 0, 2)
    incoming = lax.all_to_all(outgoing, "tp", 0, 0, tiled=False)

    both_maps = jnp.concatenate([adapter_down_maps, adapter_up_maps], axis=2)
    both_maps, outgoing = lax.optimization_barrier((both_maps, outgoing))
    column = lax.all_gather(both_maps, "z", axis=0, tiled=True)
    row_table = lax.all_gather(column, "c", axis=0, tiled=False)
    row_ids = jnp.stack(
        [slot_ids]
        + [
            lax.ppermute(slot_ids, "y", [(i, (i - shift) % y_size) for i in range(y_size)])
            for shift in range(1, y_size)
        ]
    )
    row_ids = jnp.roll(row_ids, my_row, axis=0)
    row_table, incoming = lax.optimization_barrier((row_table, incoming))

    base_result = jnp.sum(incoming, axis=0)

    sent = pick_entries(row_table, row_ids.reshape(-1), my_row, per_row, per_column)
    received = lax.all_to_all(
        sent.reshape((y_size, blocks_dev) + sent.shape[1:]), "y", 0, 0, tiled=False
    )
    chosen_maps = jnp.sum(received, axis=0, dtype=received.dtype)
    chosen_down_maps = chosen_maps[:, :, :width_dev]
    chosen_up_maps = chosen_maps[:, :, width_dev:]

    blocked_input = tokens.reshape(blocks_dev, block_rows, width_dev)
    shrunk_partial = jnp.einsum(
        "qzo,qjo->qzj", blocked_input, chosen_down_maps, preferred_element_type=jnp.float32
    ).reshape(rows_dev, rank)
    shrunk = jnp.sum(lax.all_gather(shrunk_partial, "tp", axis=0, tiled=False), axis=0)
    low_values = shrunk.astype(jnp.bfloat16)

    adapter_result = jnp.einsum(
        "bkr,brc->bkc",
        low_values.reshape(blocks_dev, block_rows, rank),
        chosen_up_maps,
        preferred_element_type=jnp.float32,
    ).reshape(rows_dev, local_columns)
    live_rows = (
        jnp.arange(block_rows, dtype=jnp.int32)[None, :] < block_live_rows[:, None]
    ).reshape(rows_dev, 1)
    adapted_output = base_result + adapter_scale * adapter_result
    return jnp.where(live_rows, adapted_output, jnp.zeros_like(adapted_output)).astype(jnp.bfloat16)


def split_mesh(mesh):
    devices = np.asarray(mesh.devices)
    first = devices[:, 0]
    y_size = len({d.coords[1] for d in first})
    z_size = len({d.coords[2] for d in first})
    c_size = len({d.core_on_chip for d in first})
    split = devices.reshape(y_size, z_size, c_size, devices.shape[1])
    for (yi, zi, ci), d in np.ndenumerate(split[:, :, :, 0]):
        assert (d.coords[1], d.coords[2], d.core_on_chip) == (
            sorted({e.coords[1] for e in first})[yi],
            sorted({e.coords[2] for e in first})[zi],
            sorted({e.core_on_chip for e in first})[ci],
        )
    return Mesh(split, ROWS + ("tp",))


def solution(mesh):
    in_specs = (
        P(ROWS, "tp"),
        P("tp", None),
        P(ROWS, None, "tp"),
        P(ROWS, None, "tp"),
        P(ROWS),
        P(ROWS),
        P(),
    )
    out_specs = P(ROWS, "tp")
    return jax.shard_map(
        shards, mesh=split_mesh(mesh), in_specs=in_specs, out_specs=out_specs, check_vma=False
    )
```

```python
import numpy as np

import jax
import jax.numpy as jnp
from jax import lax
from jax.sharding import Mesh
from jax.sharding import PartitionSpec as P

adapter_scale = 0.5
ROWS = ("y", "z", "c")


def pick_entries(table, wanted, own_row, per_row, per_column):
    row_of = wanted // per_row
    inside = wanted % per_row
    entries = table[inside % per_column, inside // per_column]
    keep = (row_of == own_row)[:, None, None]
    return jnp.where(keep, entries, jnp.zeros_like(entries))


def shards(
    tokens,
    key_value_weight,
    adapter_down_maps,
    adapter_up_maps,
    block_adapter_ids,
    block_live_rows,
    adapter_storage_slot,
):
    rows_dev, width_dev = tokens.shape
    blocks_dev = block_adapter_ids.shape[0]
    block_rows = rows_dev // blocks_dev
    rank = adapter_down_maps.shape[1]
    local_columns = adapter_up_maps.shape[2]
    tp_size = key_value_weight.shape[1] // local_columns
    y_size = lax.axis_size("y")
    per_column = lax.axis_size("c")
    per_row = lax.axis_size("z") * per_column

    slot_ids = adapter_storage_slot[block_adapter_ids]
    my_row = lax.axis_index("y")

    base_partial = jnp.dot(tokens, key_value_weight, preferred_element_type=jnp.float32)
    outgoing = base_partial.reshape(rows_dev, tp_size, local_columns).transpose(1, 0, 2)
    incoming = lax.all_to_all(outgoing, "tp", 0, 0, tiled=False)

    both_maps = jnp.concatenate([adapter_down_maps, adapter_up_maps], axis=2)
    both_maps, outgoing = lax.optimization_barrier((both_maps, outgoing))
    column = lax.all_gather(both_maps, "z", axis=0, tiled=True)
    c_size = lax.axis_size("c")
    row_table = jnp.roll(
        jnp.stack(
            [column]
            + [
                lax.ppermute(column, "c", [(i, (i + shift) % c_size) for i in range(c_size)])
                for shift in range(1, c_size)
            ]
        ),
        lax.axis_index("c"),
        axis=0,
    )
    row_ids = jnp.stack(
        [slot_ids]
        + [
            lax.ppermute(slot_ids, "y", [(i, (i - shift) % y_size) for i in range(y_size)])
            for shift in range(1, y_size)
        ]
    )
    row_ids = jnp.roll(row_ids, my_row, axis=0)
    row_table, incoming = lax.optimization_barrier((row_table, incoming))

    base_result = jnp.sum(incoming, axis=0)

    sent = pick_entries(row_table, row_ids.reshape(-1), my_row, per_row, per_column)
    received = lax.all_to_all(
        sent.reshape((y_size, blocks_dev) + sent.shape[1:]), "y", 0, 0, tiled=False
    )
    chosen_maps = jnp.sum(received, axis=0, dtype=received.dtype)
    chosen_down_maps = chosen_maps[:, :, :width_dev]
    chosen_up_maps = chosen_maps[:, :, width_dev:]

    blocked_input = tokens.reshape(blocks_dev, block_rows, width_dev)
    shrunk_partial = jnp.einsum(
        "qzo,qjo->qzj", blocked_input, chosen_down_maps, preferred_element_type=jnp.float32
    ).reshape(rows_dev, rank)
    shrunk = jnp.sum(lax.all_gather(shrunk_partial, "tp", axis=0, tiled=False), axis=0)
    low_values = shrunk.astype(jnp.bfloat16)

    adapter_result = jnp.einsum(
        "bkr,brc->bkc",
        low_values.reshape(blocks_dev, block_rows, rank),
        chosen_up_maps,
        preferred_element_type=jnp.float32,
    ).reshape(rows_dev, local_columns)
    live_rows = (
        jnp.arange(block_rows, dtype=jnp.int32)[None, :] < block_live_rows[:, None]
    ).reshape(rows_dev, 1)
    adapted_output = base_result + adapter_scale * adapter_result
    return jnp.where(live_rows, adapted_output, jnp.zeros_like(adapted_output)).astype(jnp.bfloat16)


def split_mesh(mesh):
    devices = np.asarray(mesh.devices)
    first = devices[:, 0]
    y_size = len({d.coords[1] for d in first})
    z_size = len({d.coords[2] for d in first})
    c_size = len({d.core_on_chip for d in first})
    split = devices.reshape(y_size, z_size, c_size, devices.shape[1])
    for (yi, zi, ci), d in np.ndenumerate(split[:, :, :, 0]):
        assert (d.coords[1], d.coords[2], d.core_on_chip) == (
            sorted({e.coords[1] for e in first})[yi],
            sorted({e.coords[2] for e in first})[zi],
            sorted({e.core_on_chip for e in first})[ci],
        )
    return Mesh(split, ROWS + ("tp",))


def solution(mesh):
    in_specs = (
        P(ROWS, "tp"),
        P("tp", None),
        P(ROWS, None, "tp"),
        P(ROWS, None, "tp"),
        P(ROWS),
        P(ROWS),
        P(),
    )
    out_specs = P(ROWS, "tp")
    return jax.shard_map(
        shards, mesh=split_mesh(mesh), in_specs=in_specs, out_specs=out_specs, check_vma=False
    )
```

```python
import numpy as np

import jax
import jax.numpy as jnp
from jax import lax
from jax.sharding import Mesh
from jax.sharding import PartitionSpec as P

adapter_scale = 0.5
ROWS = ("y", "zh", "zl", "c")


def pick_entries(table, wanted, own_row, per_row, per_column):
    row_of = wanted // per_row
    inside = wanted % per_row
    entries = table[inside % per_column, inside // per_column]
    keep = (row_of == own_row)[:, None, None]
    return jnp.where(keep, entries, jnp.zeros_like(entries))


def shards(
    tokens,
    key_value_weight,
    adapter_down_maps,
    adapter_up_maps,
    block_adapter_ids,
    block_live_rows,
    adapter_storage_slot,
):
    rows_dev, width_dev = tokens.shape
    blocks_dev = block_adapter_ids.shape[0]
    block_rows = rows_dev // blocks_dev
    rank = adapter_down_maps.shape[1]
    local_columns = adapter_up_maps.shape[2]
    tp_size = key_value_weight.shape[1] // local_columns
    y_size = lax.axis_size("y")
    per_column = lax.axis_size("c")
    per_row = lax.axis_size("zh") * lax.axis_size("zl") * per_column

    slot_ids = adapter_storage_slot[block_adapter_ids]
    my_row = lax.axis_index("y")

    base_partial = jnp.dot(tokens, key_value_weight, preferred_element_type=jnp.float32)
    outgoing = base_partial.reshape(rows_dev, tp_size, local_columns).transpose(1, 0, 2)
    incoming = lax.all_to_all(outgoing, "tp", 0, 0, tiled=False)

    both_maps = jnp.concatenate([adapter_down_maps, adapter_up_maps], axis=2)
    both_maps, outgoing = lax.optimization_barrier((both_maps, outgoing))
    column = lax.all_gather(both_maps, "zl", axis=0, tiled=True)
    column = lax.all_gather(column, "zh", axis=0, tiled=True)
    c_size = lax.axis_size("c")
    row_table = jnp.roll(
        jnp.stack(
            [column]
            + [
                lax.ppermute(column, "c", [(i, (i + shift) % c_size) for i in range(c_size)])
                for shift in range(1, c_size)
            ]
        ),
        lax.axis_index("c"),
        axis=0,
    )
    row_ids = jnp.stack(
        [slot_ids]
        + [
            lax.ppermute(slot_ids, "y", [(i, (i - shift) % y_size) for i in range(y_size)])
            for shift in range(1, y_size)
        ]
    )
    row_ids = jnp.roll(row_ids, my_row, axis=0)
    row_table, incoming = lax.optimization_barrier((row_table, incoming))

    base_result = jnp.sum(incoming, axis=0)

    sent = pick_entries(row_table, row_ids.reshape(-1), my_row, per_row, per_column)
    received = lax.all_to_all(
        sent.reshape((y_size, blocks_dev) + sent.shape[1:]), "y", 0, 0, tiled=False
    )
    chosen_maps = jnp.sum(received, axis=0, dtype=received.dtype)
    chosen_down_maps = chosen_maps[:, :, :width_dev]
    chosen_up_maps = chosen_maps[:, :, width_dev:]

    blocked_input = tokens.reshape(blocks_dev, block_rows, width_dev)
    shrunk_partial = jnp.einsum(
        "qzo,qjo->qzj", blocked_input, chosen_down_maps, preferred_element_type=jnp.float32
    ).reshape(rows_dev, rank)
    shrunk = jnp.sum(lax.all_gather(shrunk_partial, "tp", axis=0, tiled=False), axis=0)
    low_values = shrunk.astype(jnp.bfloat16)

    adapter_result = jnp.einsum(
        "bkr,brc->bkc",
        low_values.reshape(blocks_dev, block_rows, rank),
        chosen_up_maps,
        preferred_element_type=jnp.float32,
    ).reshape(rows_dev, local_columns)
    live_rows = (
        jnp.arange(block_rows, dtype=jnp.int32)[None, :] < block_live_rows[:, None]
    ).reshape(rows_dev, 1)
    adapted_output = base_result + adapter_scale * adapter_result
    return jnp.where(live_rows, adapted_output, jnp.zeros_like(adapted_output)).astype(jnp.bfloat16)


def split_mesh(mesh):
    devices = np.asarray(mesh.devices)
    first = devices[:, 0]
    y_size = len({d.coords[1] for d in first})
    z_size = len({d.coords[2] for d in first})
    c_size = len({d.core_on_chip for d in first})
    split = devices.reshape(y_size, z_size, c_size, devices.shape[1])
    for (yi, zi, ci), d in np.ndenumerate(split[:, :, :, 0]):
        assert (d.coords[1], d.coords[2], d.core_on_chip) == (
            sorted({e.coords[1] for e in first})[yi],
            sorted({e.coords[2] for e in first})[zi],
            sorted({e.core_on_chip for e in first})[ci],
        )
    zl_size = 4 if z_size % 4 == 0 else z_size
    split = split.reshape(y_size, z_size // zl_size, zl_size, c_size, devices.shape[1])
    return Mesh(split, ROWS + ("tp",))


def solution(mesh):
    in_specs = (
        P(ROWS, "tp"),
        P("tp", None),
        P(ROWS, None, "tp"),
        P(ROWS, None, "tp"),
        P(ROWS),
        P(ROWS),
        P(),
    )
    out_specs = P(ROWS, "tp")
    return jax.shard_map(
        shards, mesh=split_mesh(mesh), in_specs=in_specs, out_specs=out_specs, check_vma=False
    )
```

```python
import numpy as np

import jax
import jax.numpy as jnp
from jax import lax
from jax.sharding import Mesh
from jax.sharding import PartitionSpec as P

adapter_scale = 0.5
ROWS = ("y", "z", "c")


def pick_entries(table, wanted, own_row, per_row, per_column):
    row_of = wanted // per_row
    inside = wanted % per_row
    entries = table[inside % per_column, inside // per_column]
    keep = (row_of == own_row)[:, None, None]
    return jnp.where(keep, entries, jnp.zeros_like(entries))


def shards(
    tokens,
    key_value_weight,
    adapter_down_maps,
    adapter_up_maps,
    block_adapter_ids,
    block_live_rows,
    adapter_storage_slot,
):
    rows_dev, width_dev = tokens.shape
    blocks_dev = block_adapter_ids.shape[0]
    block_rows = rows_dev // blocks_dev
    rank = adapter_down_maps.shape[1]
    local_columns = adapter_up_maps.shape[2]
    tp_size = key_value_weight.shape[1] // local_columns
    y_size = lax.axis_size("y")
    per_column = lax.axis_size("c")
    per_row = lax.axis_size("z") * per_column

    slot_ids = adapter_storage_slot[block_adapter_ids]
    my_row = lax.axis_index("y")

    base_partial = jnp.dot(tokens, key_value_weight, preferred_element_type=jnp.float32)
    outgoing = base_partial.reshape(rows_dev, tp_size, local_columns).transpose(1, 0, 2)
    incoming = lax.all_to_all(outgoing, "tp", 0, 0, tiled=False)

    both_maps = jnp.concatenate([adapter_down_maps, adapter_up_maps], axis=2)
    both_maps, outgoing = lax.optimization_barrier((both_maps, outgoing))
    column = lax.all_gather(both_maps, "z", axis=0, tiled=True)
    c_size = lax.axis_size("c")
    row_table = jnp.roll(
        jnp.stack(
            [column]
            + [
                lax.ppermute(column, "c", [(i, (i + shift) % c_size) for i in range(c_size)])
                for shift in range(1, c_size)
            ]
        ),
        lax.axis_index("c"),
        axis=0,
    )
    row_ids = lax.all_to_all(
        jnp.broadcast_to(slot_ids[None], (y_size, blocks_dev)), "y", 0, 0, tiled=False
    )
    row_table, incoming = lax.optimization_barrier((row_table, incoming))

    base_result = jnp.sum(incoming, axis=0)

    sent = pick_entries(row_table, row_ids.reshape(-1), my_row, per_row, per_column)
    received = lax.all_to_all(
        sent.reshape((y_size, blocks_dev) + sent.shape[1:]), "y", 0, 0, tiled=False
    )
    chosen_maps = jnp.sum(received, axis=0, dtype=received.dtype)
    chosen_down_maps = chosen_maps[:, :, :width_dev]
    chosen_up_maps = chosen_maps[:, :, width_dev:]

    blocked_input = tokens.reshape(blocks_dev, block_rows, width_dev)
    shrunk_partial = jnp.einsum(
        "qzo,qjo->qzj", blocked_input, chosen_down_maps, preferred_element_type=jnp.float32
    ).reshape(rows_dev, rank)
    shrunk = jnp.sum(
        lax.all_to_all(
            jnp.broadcast_to(shrunk_partial[None], (tp_size,) + shrunk_partial.shape),
            "tp", 0, 0, tiled=False,
        ),
        axis=0,
    )
    low_values = shrunk.astype(jnp.bfloat16)

    adapter_result = jnp.einsum(
        "bkr,brc->bkc",
        low_values.reshape(blocks_dev, block_rows, rank),
        chosen_up_maps,
        preferred_element_type=jnp.float32,
    ).reshape(rows_dev, local_columns)
    live_rows = (
        jnp.arange(block_rows, dtype=jnp.int32)[None, :] < block_live_rows[:, None]
    ).reshape(rows_dev, 1)
    adapted_output = base_result + adapter_scale * adapter_result
    return jnp.where(live_rows, adapted_output, jnp.zeros_like(adapted_output)).astype(jnp.bfloat16)


def split_mesh(mesh):
    devices = np.asarray(mesh.devices)
    first = devices[:, 0]
    y_size = len({d.coords[1] for d in first})
    z_size = len({d.coords[2] for d in first})
    c_size = len({d.core_on_chip for d in first})
    split = devices.reshape(y_size, z_size, c_size, devices.shape[1])
    for (yi, zi, ci), d in np.ndenumerate(split[:, :, :, 0]):
        assert (d.coords[1], d.coords[2], d.core_on_chip) == (
            sorted({e.coords[1] for e in first})[yi],
            sorted({e.coords[2] for e in first})[zi],
            sorted({e.core_on_chip for e in first})[ci],
        )
    return Mesh(split, ROWS + ("tp",))


def solution(mesh):
    in_specs = (
        P(ROWS, "tp"),
        P("tp", None),
        P(ROWS, None, "tp"),
        P(ROWS, None, "tp"),
        P(ROWS),
        P(ROWS),
        P(),
    )
    out_specs = P(ROWS, "tp")
    return jax.shard_map(
        shards, mesh=split_mesh(mesh), in_specs=in_specs, out_specs=out_specs, check_vma=False
    )
```

```python
import numpy as np

import jax
import jax.numpy as jnp
from jax import lax
from jax.sharding import Mesh
from jax.sharding import PartitionSpec as P

adapter_scale = 0.5
ROWS = ("y", "z", "c")


def pick_entries(table, wanted, own_row, per_row, per_column):
    row_of = wanted // per_row
    inside = wanted % per_row
    entries = table[inside % per_column, inside // per_column]
    keep = (row_of == own_row)[:, None, None]
    return jnp.where(keep, entries, jnp.zeros_like(entries))


def shards(
    tokens,
    key_value_weight,
    adapter_down_maps,
    adapter_up_maps,
    block_adapter_ids,
    block_live_rows,
    adapter_storage_slot,
):
    rows_dev, width_dev = tokens.shape
    blocks_dev = block_adapter_ids.shape[0]
    block_rows = rows_dev // blocks_dev
    rank = adapter_down_maps.shape[1]
    local_columns = adapter_up_maps.shape[2]
    tp_size = key_value_weight.shape[1] // local_columns
    y_size = lax.axis_size("y")
    per_column = lax.axis_size("c")
    per_row = lax.axis_size("z") * per_column

    slot_ids = adapter_storage_slot[block_adapter_ids]
    my_row = lax.axis_index("y")

    base_partial = jnp.dot(tokens, key_value_weight, preferred_element_type=jnp.float32)
    peak = jnp.max(jnp.abs(base_partial))
    exponent = jnp.clip(jnp.floor(jnp.log2(jnp.maximum(peak, 1e-30))), -100.0, 100.0)
    scaled = (base_partial * jnp.exp2(13.0 - exponent)).astype(jnp.float16)
    outgoing = jnp.concatenate(
        [
            scaled.reshape(rows_dev, tp_size, local_columns).transpose(1, 0, 2),
            jnp.broadcast_to(exponent.astype(jnp.float16), (tp_size, 16, local_columns)),
        ],
        axis=1,
    )
    incoming = lax.all_to_all(outgoing, "tp", 0, 0, tiled=False)

    both_maps = jnp.concatenate([adapter_down_maps, adapter_up_maps], axis=2)
    both_maps, outgoing = lax.optimization_barrier((both_maps, outgoing))
    column = lax.all_gather(both_maps, "z", axis=0, tiled=True)
    c_size = lax.axis_size("c")
    row_table = jnp.roll(
        jnp.stack(
            [column]
            + [
                lax.ppermute(column, "c", [(i, (i + shift) % c_size) for i in range(c_size)])
                for shift in range(1, c_size)
            ]
        ),
        lax.axis_index("c"),
        axis=0,
    )
    row_ids = lax.all_to_all(
        jnp.broadcast_to(slot_ids[None], (y_size, blocks_dev)), "y", 0, 0, tiled=False
    )
    row_table, incoming = lax.optimization_barrier((row_table, incoming))

    unscale = jnp.exp2(incoming[:, rows_dev, 0].astype(jnp.float32) - 13.0)
    base_result = jnp.sum(
        incoming[:, :rows_dev].astype(jnp.float32) * unscale[:, None, None], axis=0
    )

    sent = pick_entries(row_table, row_ids.reshape(-1), my_row, per_row, per_column)
    received = lax.all_to_all(
        sent.reshape((y_size, blocks_dev) + sent.shape[1:]), "y", 0, 0, tiled=False
    )
    chosen_maps = jnp.sum(received, axis=0, dtype=received.dtype)
    chosen_down_maps = chosen_maps[:, :, :width_dev]
    chosen_up_maps = chosen_maps[:, :, width_dev:]

    blocked_input = tokens.reshape(blocks_dev, block_rows, width_dev)
    shrunk_partial = jnp.einsum(
        "qzo,qjo->qzj", blocked_input, chosen_down_maps, preferred_element_type=jnp.float32
    ).reshape(rows_dev, rank)
    shrunk = jnp.sum(
        lax.all_to_all(
            jnp.broadcast_to(shrunk_partial[None], (tp_size,) + shrunk_partial.shape),
            "tp", 0, 0, tiled=False,
        ),
        axis=0,
    )
    low_values = shrunk.astype(jnp.bfloat16)

    adapter_result = jnp.einsum(
        "bkr,brc->bkc",
        low_values.reshape(blocks_dev, block_rows, rank),
        chosen_up_maps,
        preferred_element_type=jnp.float32,
    ).reshape(rows_dev, local_columns)
    live_rows = (
        jnp.arange(block_rows, dtype=jnp.int32)[None, :] < block_live_rows[:, None]
    ).reshape(rows_dev, 1)
    adapted_output = base_result + adapter_scale * adapter_result
    return jnp.where(live_rows, adapted_output, jnp.zeros_like(adapted_output)).astype(jnp.bfloat16)


def split_mesh(mesh):
    devices = np.asarray(mesh.devices)
    first = devices[:, 0]
    y_size = len({d.coords[1] for d in first})
    z_size = len({d.coords[2] for d in first})
    c_size = len({d.core_on_chip for d in first})
    split = devices.reshape(y_size, z_size, c_size, devices.shape[1])
    for (yi, zi, ci), d in np.ndenumerate(split[:, :, :, 0]):
        assert (d.coords[1], d.coords[2], d.core_on_chip) == (
            sorted({e.coords[1] for e in first})[yi],
            sorted({e.coords[2] for e in first})[zi],
            sorted({e.core_on_chip for e in first})[ci],
        )
    return Mesh(split, ROWS + ("tp",))


def solution(mesh):
    in_specs = (
        P(ROWS, "tp"),
        P("tp", None),
        P(ROWS, None, "tp"),
        P(ROWS, None, "tp"),
        P(ROWS),
        P(ROWS),
        P(),
    )
    out_specs = P(ROWS, "tp")
    return jax.shard_map(
        shards, mesh=split_mesh(mesh), in_specs=in_specs, out_specs=out_specs, check_vma=False
    )
```

```python
import numpy as np

import jax
import jax.numpy as jnp
from jax import lax
from jax.sharding import Mesh
from jax.sharding import PartitionSpec as P

adapter_scale = 0.5
ROWS = ("y", "z", "c")


def pick_entries(table, wanted, own_row, own_column, per_row, per_column):
    row_of = wanted // per_row
    inside = wanted % per_row
    entries = table[(own_column - inside % per_column) % per_column, inside // per_column]
    keep = (row_of == own_row)[:, None, None]
    return jnp.where(keep, entries, jnp.zeros_like(entries))


def shards(
    tokens,
    key_value_weight,
    adapter_down_maps,
    adapter_up_maps,
    block_adapter_ids,
    block_live_rows,
    adapter_storage_slot,
):
    rows_dev, width_dev = tokens.shape
    blocks_dev = block_adapter_ids.shape[0]
    block_rows = rows_dev // blocks_dev
    rank = adapter_down_maps.shape[1]
    local_columns = adapter_up_maps.shape[2]
    tp_size = key_value_weight.shape[1] // local_columns
    y_size = lax.axis_size("y")
    per_column = lax.axis_size("c")
    per_row = lax.axis_size("z") * per_column

    slot_ids = adapter_storage_slot[block_adapter_ids]
    my_row = lax.axis_index("y")

    base_partial = jnp.dot(tokens, key_value_weight, preferred_element_type=jnp.float32)
    outgoing = base_partial.reshape(rows_dev, tp_size, local_columns).transpose(1, 0, 2)
    incoming = lax.all_to_all(outgoing, "tp", 0, 0, tiled=False)

    both_maps = jnp.concatenate([adapter_down_maps, adapter_up_maps], axis=2)
    both_maps, outgoing = lax.optimization_barrier((both_maps, outgoing))
    column = lax.all_gather(both_maps, "z", axis=0, tiled=True)
    c_size = lax.axis_size("c")
    row_table = jnp.stack(
        [column]
        + [
            lax.ppermute(column, "c", [(i, (i + shift) % c_size) for i in range(c_size)])
            for shift in range(1, c_size)
        ]
    )
    row_ids = lax.all_to_all(
        jnp.broadcast_to(slot_ids[None], (y_size, blocks_dev)), "y", 0, 0, tiled=False
    )
    row_table, incoming = lax.optimization_barrier((row_table, incoming))

    base_result = jnp.sum(incoming, axis=0)

    sent = pick_entries(
        row_table, row_ids.reshape(-1), my_row, lax.axis_index("c"), per_row, per_column
    )
    received = lax.all_to_all(
        sent.reshape((y_size, blocks_dev) + sent.shape[1:]), "y", 0, 0, tiled=False
    )
    chosen_maps = jnp.sum(received, axis=0, dtype=received.dtype)
    chosen_down_maps = chosen_maps[:, :, :width_dev]
    chosen_up_maps = chosen_maps[:, :, width_dev:]

    blocked_input = tokens.reshape(blocks_dev, block_rows, width_dev)
    shrunk_partial = jnp.einsum(
        "qzo,qjo->qzj", blocked_input, chosen_down_maps, preferred_element_type=jnp.float32
    ).reshape(rows_dev, rank)
    shrunk = jnp.sum(
        lax.all_to_all(
            jnp.broadcast_to(shrunk_partial[None], (tp_size,) + shrunk_partial.shape),
            "tp", 0, 0, tiled=False,
        ),
        axis=0,
    )
    low_values = shrunk.astype(jnp.bfloat16)

    adapter_result = jnp.einsum(
        "bkr,brc->bkc",
        low_values.reshape(blocks_dev, block_rows, rank),
        chosen_up_maps,
        preferred_element_type=jnp.float32,
    ).reshape(rows_dev, local_columns)
    live_rows = (
        jnp.arange(block_rows, dtype=jnp.int32)[None, :] < block_live_rows[:, None]
    ).reshape(rows_dev, 1)
    adapted_output = base_result + adapter_scale * adapter_result
    return jnp.where(live_rows, adapted_output, jnp.zeros_like(adapted_output)).astype(jnp.bfloat16)


def split_mesh(mesh):
    devices = np.asarray(mesh.devices)
    first = devices[:, 0]
    y_size = len({d.coords[1] for d in first})
    z_size = len({d.coords[2] for d in first})
    c_size = len({d.core_on_chip for d in first})
    split = devices.reshape(y_size, z_size, c_size, devices.shape[1])
    for (yi, zi, ci), d in np.ndenumerate(split[:, :, :, 0]):
        assert (d.coords[1], d.coords[2], d.core_on_chip) == (
            sorted({e.coords[1] for e in first})[yi],
            sorted({e.coords[2] for e in first})[zi],
            sorted({e.core_on_chip for e in first})[ci],
        )
    return Mesh(split, ROWS + ("tp",))


def solution(mesh):
    in_specs = (
        P(ROWS, "tp"),
        P("tp", None),
        P(ROWS, None, "tp"),
        P(ROWS, None, "tp"),
        P(ROWS),
        P(ROWS),
        P(),
    )
    out_specs = P(ROWS, "tp")
    return jax.shard_map(
        shards, mesh=split_mesh(mesh), in_specs=in_specs, out_specs=out_specs, check_vma=False
    )
```

```python
import numpy as np

import jax
import jax.numpy as jnp
from jax import lax
from jax.experimental.layout import Layout, with_layout_constraint
from jax.sharding import Mesh
from jax.sharding import PartitionSpec as P

adapter_scale = 0.5
ROWS = ("y", "z", "c")


def pick_entries(table, wanted, own_row, own_column, per_row, per_column):
    row_of = wanted // per_row
    inside = wanted % per_row
    entries = table[(own_column - inside % per_column) % per_column, inside // per_column]
    keep = (row_of == own_row)[:, None, None]
    return jnp.where(keep, entries, jnp.zeros_like(entries))


def shards(
    tokens,
    key_value_weight,
    adapter_down_maps,
    adapter_up_maps,
    block_adapter_ids,
    block_live_rows,
    adapter_storage_slot,
):
    rows_dev, width_dev = tokens.shape
    blocks_dev = block_adapter_ids.shape[0]
    block_rows = rows_dev // blocks_dev
    rank = adapter_down_maps.shape[1]
    local_columns = adapter_up_maps.shape[2]
    tp_size = key_value_weight.shape[1] // local_columns
    y_size = lax.axis_size("y")
    per_column = lax.axis_size("c")
    per_row = lax.axis_size("z") * per_column

    slot_ids = adapter_storage_slot[block_adapter_ids]
    my_row = lax.axis_index("y")

    base_partial = jnp.dot(tokens, key_value_weight, preferred_element_type=jnp.float32)
    outgoing = base_partial.reshape(rows_dev, tp_size, local_columns).transpose(1, 0, 2)
    incoming = lax.all_to_all(outgoing, "tp", 0, 0, tiled=False)

    both_maps = jnp.concatenate([adapter_down_maps, adapter_up_maps], axis=2)
    both_maps, outgoing = lax.optimization_barrier((both_maps, outgoing))
    column = lax.all_gather(both_maps, "z", axis=0, tiled=True)
    c_size = lax.axis_size("c")
    row_table = jnp.stack(
        [column]
        + [
            lax.ppermute(column, "c", [(i, (i + shift) % c_size) for i in range(c_size)])
            for shift in range(1, c_size)
        ]
    )
    row_ids = lax.all_to_all(
        jnp.broadcast_to(slot_ids[None], (y_size, blocks_dev)), "y", 0, 0, tiled=False
    )
    row_table, incoming = lax.optimization_barrier((row_table, incoming))

    base_result = with_layout_constraint(jnp.sum(incoming, axis=0), Layout((0, 1)))

    sent = pick_entries(
        row_table, row_ids.reshape(-1), my_row, lax.axis_index("c"), per_row, per_column
    )
    received = lax.all_to_all(
        sent.reshape((y_size, blocks_dev) + sent.shape[1:]), "y", 0, 0, tiled=False
    )
    chosen_maps = jnp.sum(received, axis=0, dtype=received.dtype)
    chosen_down_maps = chosen_maps[:, :, :width_dev]
    chosen_up_maps = chosen_maps[:, :, width_dev:]

    blocked_input = tokens.reshape(blocks_dev, block_rows, width_dev)
    shrunk_partial = jnp.einsum(
        "qzo,qjo->qzj", blocked_input, chosen_down_maps, preferred_element_type=jnp.float32
    ).reshape(rows_dev, rank)
    shrunk = jnp.sum(
        lax.all_to_all(
            jnp.broadcast_to(shrunk_partial[None], (tp_size,) + shrunk_partial.shape),
            "tp", 0, 0, tiled=False,
        ),
        axis=0,
    )
    low_values = shrunk.astype(jnp.bfloat16)

    adapter_result = jnp.einsum(
        "bkr,brc->bkc",
        low_values.reshape(blocks_dev, block_rows, rank),
        chosen_up_maps,
        preferred_element_type=jnp.float32,
    ).reshape(rows_dev, local_columns)
    live_rows = (
        jnp.arange(block_rows, dtype=jnp.int32)[None, :] < block_live_rows[:, None]
    ).reshape(rows_dev, 1)
    adapted_output = base_result + adapter_scale * adapter_result
    return jnp.where(live_rows, adapted_output, jnp.zeros_like(adapted_output)).astype(jnp.bfloat16)


def split_mesh(mesh):
    devices = np.asarray(mesh.devices)
    first = devices[:, 0]
    y_size = len({d.coords[1] for d in first})
    z_size = len({d.coords[2] for d in first})
    c_size = len({d.core_on_chip for d in first})
    split = devices.reshape(y_size, z_size, c_size, devices.shape[1])
    for (yi, zi, ci), d in np.ndenumerate(split[:, :, :, 0]):
        assert (d.coords[1], d.coords[2], d.core_on_chip) == (
            sorted({e.coords[1] for e in first})[yi],
            sorted({e.coords[2] for e in first})[zi],
            sorted({e.core_on_chip for e in first})[ci],
        )
    return Mesh(split, ROWS + ("tp",))


def solution(mesh):
    in_specs = (
        P(ROWS, "tp"),
        P("tp", None),
        P(ROWS, None, "tp"),
        P(ROWS, None, "tp"),
        P(ROWS),
        P(ROWS),
        P(),
    )
    out_specs = P(ROWS, "tp")
    return jax.shard_map(
        shards, mesh=split_mesh(mesh), in_specs=in_specs, out_specs=out_specs, check_vma=False
    )
```

```python
import numpy as np

import jax
import jax.numpy as jnp
from jax import lax
from jax.experimental.layout import Layout, with_layout_constraint
from jax.sharding import Mesh
from jax.sharding import PartitionSpec as P

adapter_scale = 0.5
ROWS = ("y", "z", "c")


def pick_entries(table, wanted, own_row, own_column, per_row, per_column):
    row_of = wanted // per_row
    inside = wanted % per_row
    entries = table[(own_column - inside % per_column) % per_column, inside // per_column]
    keep = (row_of == own_row)[:, None, None]
    return jnp.where(keep, entries, jnp.zeros_like(entries))


def shards(
    tokens,
    key_value_weight,
    adapter_down_maps,
    adapter_up_maps,
    block_adapter_ids,
    block_live_rows,
    adapter_storage_slot,
):
    rows_dev, width_dev = tokens.shape
    blocks_dev = block_adapter_ids.shape[0]
    block_rows = rows_dev // blocks_dev
    rank = adapter_down_maps.shape[1]
    local_columns = adapter_up_maps.shape[2]
    tp_size = key_value_weight.shape[1] // local_columns
    y_size = lax.axis_size("y")
    per_column = lax.axis_size("c")
    per_row = lax.axis_size("z") * per_column

    slot_ids = adapter_storage_slot[block_adapter_ids]
    my_row = lax.axis_index("y")

    base_partial = jnp.dot(tokens, key_value_weight, preferred_element_type=jnp.float32)
    outgoing = base_partial.reshape(rows_dev, tp_size, local_columns).transpose(1, 0, 2)
    incoming = lax.all_to_all(outgoing, "tp", 0, 0, tiled=False)

    both_maps = jnp.concatenate([adapter_down_maps, adapter_up_maps], axis=2)
    both_maps, outgoing = lax.optimization_barrier((both_maps, outgoing))
    column = lax.all_gather(both_maps, "z", axis=0, tiled=True)
    c_size = lax.axis_size("c")
    row_table = jnp.stack(
        [column]
        + [
            lax.ppermute(column, "c", [(i, (i + shift) % c_size) for i in range(c_size)])
            for shift in range(1, c_size)
        ]
    )
    row_ids = lax.all_to_all(
        jnp.broadcast_to(slot_ids[None], (y_size, blocks_dev)), "y", 0, 0, tiled=False
    )
    row_table, incoming = lax.optimization_barrier((row_table, incoming))

    base_result = with_layout_constraint(jnp.sum(incoming, axis=0), Layout((0, 1)))

    sent = pick_entries(
        row_table, row_ids.reshape(-1), my_row, lax.axis_index("c"), per_row, per_column
    )
    received = lax.all_to_all(
        sent.reshape((y_size, blocks_dev) + sent.shape[1:]), "y", 0, 0, tiled=False
    )
    received, base_result = lax.optimization_barrier((received, base_result))
    chosen_maps = jnp.sum(received, axis=0, dtype=received.dtype)
    chosen_down_maps = chosen_maps[:, :, :width_dev]
    chosen_up_maps = chosen_maps[:, :, width_dev:]

    blocked_input = tokens.reshape(blocks_dev, block_rows, width_dev)
    shrunk_partial = jnp.einsum(
        "qzo,qjo->qzj", blocked_input, chosen_down_maps, preferred_element_type=jnp.float32
    ).reshape(rows_dev, rank)
    shrunk = jnp.sum(
        lax.all_to_all(
            jnp.broadcast_to(shrunk_partial[None], (tp_size,) + shrunk_partial.shape),
            "tp", 0, 0, tiled=False,
        ),
        axis=0,
    )
    low_values = shrunk.astype(jnp.bfloat16)

    adapter_result = jnp.einsum(
        "bkr,brc->bkc",
        low_values.reshape(blocks_dev, block_rows, rank),
        chosen_up_maps,
        preferred_element_type=jnp.float32,
    ).reshape(rows_dev, local_columns)
    live_rows = (
        jnp.arange(block_rows, dtype=jnp.int32)[None, :] < block_live_rows[:, None]
    ).reshape(rows_dev, 1)
    adapted_output = base_result + adapter_scale * adapter_result
    return jnp.where(live_rows, adapted_output, jnp.zeros_like(adapted_output)).astype(jnp.bfloat16)


def split_mesh(mesh):
    devices = np.asarray(mesh.devices)
    first = devices[:, 0]
    y_size = len({d.coords[1] for d in first})
    z_size = len({d.coords[2] for d in first})
    c_size = len({d.core_on_chip for d in first})
    split = devices.reshape(y_size, z_size, c_size, devices.shape[1])
    for (yi, zi, ci), d in np.ndenumerate(split[:, :, :, 0]):
        assert (d.coords[1], d.coords[2], d.core_on_chip) == (
            sorted({e.coords[1] for e in first})[yi],
            sorted({e.coords[2] for e in first})[zi],
            sorted({e.core_on_chip for e in first})[ci],
        )
    return Mesh(split, ROWS + ("tp",))


def solution(mesh):
    in_specs = (
        P(ROWS, "tp"),
        P("tp", None),
        P(ROWS, None, "tp"),
        P(ROWS, None, "tp"),
        P(ROWS),
        P(ROWS),
        P(),
    )
    out_specs = P(ROWS, "tp")
    return jax.shard_map(
        shards, mesh=split_mesh(mesh), in_specs=in_specs, out_specs=out_specs, check_vma=False
    )
```
